128 devices in a mesh: gx: 16 (over x_hi, z, core), gy: 8 (over x_lo, y).
Axes of the slice: x: 4 (x_hi: 2, x_lo: 2; x = x_hi * 2 + x_lo), y: 4, z: 4, core: 2. Of those that a mesh axis runs over, the one named last changes fastest.
Arguments:
- patches: bfloat16 [8, 64, 256, 1024], P(None, None, 'gx', 'gy'), may hold values from -6 to 6
- patch_wx: bfloat16 [8, 8, 256], P(None, 'gy', 'gx'), may hold values from 1 to 3
- patch_wy: bfloat16 [8, 16, 1024], P(None, 'gx', 'gy'), may hold values from 1 to 3
- offset_x: int32 [8, 16, 8], P(None, 'gx', 'gy'), may hold values from 0 to 15
- offset_y: int32 [8, 16, 8], P(None, 'gx', 'gy'), may hold values from 0 to 127
- block_counts: int32 [16, 8], P('gx', 'gy'), may hold values from 2 to 8, as said below
- template: bfloat16 [64, 256, 1024], P(None, 'gx', 'gy'), may hold values from -6 to 6
- stiff_mu: float32 [64, 256, 1024], P(None, 'gx', 'gy'), may hold values from 0.5 to 2
- stiff_lam: float32 [64, 256, 1024], P(None, 'gx', 'gy'), may hold values from 0.5 to 4
- start_field: float32 [3, 64, 256, 1024], P(None, None, 'gx', 'gy'), may hold values from -4 to 4
Outputs:
- joined: bfloat16 [64, 256, 1024], P(None, 'gx', 'gy')
- field: float32 [3, 64, 256, 1024], P(None, None, 'gx', 'gy')
The draws below stay inside these ranges and needn't reach their ends.
Inputs may be any that keep to these rules, and one draw needn't show every extreme that they name: `block_counts`: a block's patch slots at or beyond its count are unused; some block holds exactly 8 live patches.
All inputs are finite; a program needn't handle non-finite values.
Results may differ from the reference program's by a relative error of at most 0.0045.
Values may be sent and summed in bfloat16 or wider, within the bound.
No kernel may reach another device: no remote copies, remote signals or barrier semaphores. Data moves between devices by JAX's collectives and lax.ppermute only.
A program may use at most 128 MiB of HBM per device.

```python
import math
import jax
import jax.numpy as jnp
from jax import lax

BX = 16
BY = 128
Z = 64
SLOTS = 8
PASSES = 4
NX = 256
NY = 1024
N_GX = 16
N_GY = 8


def draw_block_counts(key, part):
    key_base, key_heavy, key_pick = jax.random.split(key, 3)
    base_count = jax.random.randint(key_base, (N_GX, N_GY), 2, SLOTS // 2 + 2)
    heavy = jax.random.randint(key_heavy, (N_GX, N_GY), 0, 8) == 0
    chosen = jax.random.randint(key_pick, (), 0, N_GX * N_GY)
    position = jnp.arange(N_GX * N_GY).reshape(N_GX, N_GY)
    filled = heavy | (position == chosen)
    return jnp.where(filled, SLOTS, jnp.minimum(base_count, SLOTS)).astype(jnp.int32)


def touch_ends(entries, own_key, low, top_value):
    longest = entries.shape.index(max(entries.shape))
    spots = []
    for shift in (0, 1):
        where = [jax.random.randint(jax.random.fold_in(own_key, axis), (), 0, length) for axis, length in enumerate(entries.shape)]
        where[longest] = (where[longest] + shift) % entries.shape[longest]
        spots.append(tuple(where))
    return entries.at[spots[0]].set(low).at[spots[1]].set(top_value)


def block_scale(key, extent, pieces, low, largest):
    level, own = 1.0, jax.random.fold_in(key, 6)
    for dim, blocks in pieces:
        heights = jnp.exp(jax.random.uniform(jax.random.fold_in(own, dim), (blocks,), jnp.float32, low / len(pieces), largest / len(pieces)))
        level = level * jnp.repeat(heights, extent[dim] // blocks).reshape([-1 if axis == dim else 1 for axis in range(len(extent))])
    return level


def gaussian(rng, dims, width, limit, shards=(), held_as=jnp.bfloat16):
    array = width * jax.random.normal(rng, dims, jnp.float32)
    if shards:
        array = array * block_scale(rng, dims, shards, -0.22, 0.18)
    return jnp.clip(array, -limit, limit).astype(held_as)


def setup_inputs(seed: int = 0) -> dict:
    streams_of = jax.random.split(jax.random.key(seed), 11)
    patches = gaussian(streams_of[0], (SLOTS, Z, NX, NY), 1.0, 6.0, ((2, 16), (3, 8)))
    patch_wx = jnp.clip(jnp.exp(math.log(3.0) - 1.0986123 * jax.random.uniform(streams_of[1], (SLOTS, N_GY, NX), jnp.float32) ** block_scale(streams_of[1], (SLOTS, N_GY, NX), ((1, 8), (2, 16)), -0.2, 0.2)), 1.0, 3.0).astype(jnp.bfloat16)
    patch_wy = jnp.clip(jnp.exp(math.log(3.0) - 1.0986123 * jax.random.uniform(streams_of[2], (SLOTS, N_GX, NY), jnp.float32) ** block_scale(streams_of[2], (SLOTS, N_GX, NY), ((1, 16), (2, 8)), -0.2, 0.2)), 1.0, 3.0).astype(jnp.bfloat16)
    offset_x = touch_ends(jax.random.randint(streams_of[3], (SLOTS, N_GX, N_GY), 0, BX), jax.random.fold_in(streams_of[3], 1), 0, BX - 1).astype(jnp.int32)
    offset_y = touch_ends(jax.random.randint(streams_of[4], (SLOTS, N_GX, N_GY), 0, BY), jax.random.fold_in(streams_of[4], 1), 0, BY - 1).astype(jnp.int32)
    block_counts = draw_block_counts(jax.random.fold_in(streams_of[10], 71), 0)
    template = gaussian(streams_of[6], (Z, NX, NY), 1.0, 6.0, ((1, 16), (2, 8)))
    stiff_mu = jnp.clip(jnp.exp(math.log(2.0) - 1.3862944 * jax.random.uniform(streams_of[7], (Z, NX, NY), jnp.float32) ** block_scale(streams_of[7], (Z, NX, NY), ((1, 16), (2, 8)), -0.2, 0.2)), 0.5, 2.0)
    stiff_lam = jnp.clip(jnp.exp(math.log(4.0) - 2.0794415 * jax.random.uniform(streams_of[8], (Z, NX, NY), jnp.float32) ** block_scale(streams_of[8], (Z, NX, NY), ((1, 16), (2, 8)), -0.2, 0.2)), 0.5, 4.0)
    start_field = gaussian(streams_of[9], (3, Z, NX, NY), 0.5, 4.0, ((2, 16), (3, 8)), jnp.float32)
    return dict(patches=patches, patch_wx=patch_wx, patch_wy=patch_wy, offset_x=offset_x, offset_y=offset_y, block_counts=block_counts, template=template, stiff_mu=stiff_mu, stiff_lam=stiff_lam, start_field=start_field)


RELAX_FACTOR = 0.9
STEPS_UNIT = ((1, 0, 0), (0, 1, 0), (0, 0, 1))


def window(array_in, move_z, move_x, move_y):
    size_z = array_in.shape[-3] - 4
    size_x = array_in.shape[-2] - 4
    size_y = array_in.shape[-1] - 4
    return array_in[..., 2 + move_z:2 + move_z + size_z, 2 + move_x:2 + move_x + size_x, 2 + move_y:2 + move_y + size_y]


def moved(base, step_dir, factor):
    return (base[0] + factor * step_dir[0], base[1] + factor * step_dir[1], base[2] + factor * step_dir[2])


def divergence(padded, at_pos):
    result = 0.0
    for dim_idx in range(3):
        ahead = moved(at_pos, STEPS_UNIT[dim_idx], 1)
        behind = moved(at_pos, STEPS_UNIT[dim_idx], -1)
        result = result + 0.5 * (window(padded[dim_idx], *ahead) - window(padded[dim_idx], *behind))
    return result


def relax_pass(padded, shear, bulk, rate, forcing):
    shear_here = window(shear, 0, 0, 0)
    updated = []
    for comp_idx in range(3):
        values = padded[comp_idx]
        centre = window(values, 0, 0, 0)
        laplace = 0.0
        for dim_idx in range(3):
            ahead = STEPS_UNIT[dim_idx]
            behind = moved((0, 0, 0), ahead, -1)
            laplace = laplace + 0.5 * (shear_here + window(shear, *ahead)) * (window(values, *ahead) - centre)
            laplace = laplace - 0.5 * (shear_here + window(shear, *behind)) * (centre - window(values, *behind))
        ahead = STEPS_UNIT[comp_idx]
        behind = moved((0, 0, 0), ahead, -1)
        grad_div = 0.5 * (window(bulk, *ahead) * divergence(padded, ahead) - window(bulk, *behind) * divergence(padded, behind))
        updated.append(centre + rate * (laplace + grad_div + forcing[comp_idx]))
    return jnp.stack(updated)


def force_field(images):
    joined_ext = images[0].astype(jnp.float32)
    template_ext = images[1].astype(jnp.float32)
    centre = joined_ext[:, 1:-1, 1:-1]
    mismatch = template_ext[:, 1:-1, 1:-1] - centre
    padded_z = jnp.pad(centre, ((1, 1), (0, 0), (0, 0)))
    slope_z = 0.5 * (padded_z[2:] - padded_z[:-2])
    slope_x = 0.5 * (joined_ext[:, 2:, 1:-1] - joined_ext[:, :-2, 1:-1])
    slope_y = 0.5 * (joined_ext[:, 1:-1, 2:] - joined_ext[:, 1:-1, :-2])
    return jnp.stack([slope_z * mismatch, slope_x * mismatch, slope_y * mismatch])


def reference(patches, patch_wx, patch_wy, offset_x, offset_y, block_counts, template, stiff_mu, stiff_lam, start_field):
    def add_patch(flat, carry):
        weighted, weight_sum = carry
        flat = flat.astype(jnp.int32)
        col_i = flat // (N_GY * SLOTS)
        row_j = (flat // SLOTS) % N_GY
        slot_idx = flat % SLOTS
        start_x = (col_i * BX + offset_x[slot_idx, col_i, row_j]).astype(jnp.int32)
        start_y = (row_j * BY + offset_y[slot_idx, col_i, row_j]).astype(jnp.int32)
        zero_idx = jnp.zeros((), jnp.int32)
        piece = lax.dynamic_slice(patches, (slot_idx, zero_idx, (col_i * BX).astype(jnp.int32), (row_j * BY).astype(jnp.int32)), (1, Z, BX, BY))[0]
        along_x = lax.dynamic_slice(patch_wx, (slot_idx, row_j, (col_i * BX).astype(jnp.int32)), (1, 1, BX))[0, 0].astype(jnp.float32)
        along_y = lax.dynamic_slice(patch_wy, (slot_idx, col_i, (row_j * BY).astype(jnp.int32)), (1, 1, BY))[0, 0].astype(jnp.float32)
        live = (slot_idx < block_counts[col_i, row_j]).astype(jnp.float32)
        weights = along_x[:, None] * along_y[None, :] * live
        region = lax.dynamic_slice(weighted, (zero_idx, start_x, start_y), (Z, BX, BY))
        weighted = lax.dynamic_update_slice(weighted, region + piece.astype(jnp.float32) * weights[None], (zero_idx, start_x, start_y))
        plane = lax.dynamic_slice(weight_sum, (start_x, start_y), (BX, BY))
        weight_sum = lax.dynamic_update_slice(weight_sum, plane + weights, (start_x, start_y))
        return weighted, weight_sum

    initial = (jnp.zeros((Z, NX + BX, NY + BY), jnp.float32), jnp.zeros((NX + BX, NY + BY), jnp.float32))
    weighted, weight_sum = lax.fori_loop(0, N_GX * N_GY * SLOTS, add_patch, initial)
    joined = (weighted[:, :NX, :NY] / jnp.maximum(weight_sum[:NX, :NY], 1.0)[None]).astype(jnp.bfloat16)
    bulk = stiff_lam + stiff_mu
    rate = RELAX_FACTOR / (6.0 * stiff_mu + 3.0 * bulk)
    images = jnp.pad(jnp.stack([joined, template]), ((0, 0), (0, 0), (1, 1), (1, 1)))
    forcing = force_field(images)
    shear_pad = jnp.pad(stiff_mu, 2)
    bulk_pad = jnp.pad(bulk, 2)
    field = start_field
    for pass_idx in range(PASSES):
        widened = jnp.pad(field, ((0, 0), (2, 2), (2, 2), (2, 2)))
        field = relax_pass(widened, shear_pad, bulk_pad, rate, forcing)
    return joined, field
```

```python
import jax
import jax.numpy as jnp
from jax import lax
from jax.experimental import pallas as pl
from jax.experimental.pallas import tpu as pltpu
from jax.sharding import PartitionSpec as P

PASSES = 4


RELAX_FACTOR = 0.9
STEPS_UNIT = ((1, 0, 0), (0, 1, 0), (0, 0, 1))
EXACT = lax.Precision.HIGHEST
HALF = 8


def shifted_in(block, axis, distance):
    count = lax.axis_size(axis)
    route = [(i, i + distance) for i in range(count) if 0 <= i + distance < count]
    return lax.ppermute(block, axis, route)


def diagonal_in(block):
    nx = lax.axis_size("gx")
    ny = lax.axis_size("gy")
    route = [(i * ny + j, (i + 1) * ny + j + 1) for i in range(nx - 1) for j in range(ny - 1)]
    return lax.ppermute(block, ("gx", "gy"), route)


def halo(v):
    chans, depth, wide_x, wide_y = v.shape
    y_low = shifted_in(v[..., wide_y - 2 :], "gy", 1)
    y_high = shifted_in(v[..., :2], "gy", -1)
    wrapped = jnp.concatenate(
        [y_high, jnp.zeros((chans, depth, wide_x, wide_y - 4), v.dtype), y_low], axis=-1
    )
    upward = jnp.concatenate([v[:, :, wide_x - 2 :], wrapped[:, :, wide_x - 2 :]], axis=2)
    downward = jnp.concatenate([v[:, :, :2], wrapped[:, :, :2]], axis=2)
    x_low = shifted_in(upward, "gx", 1)
    x_high = shifted_in(downward, "gx", -1)
    z_pad = ((0, 0), (2, 2), (0, 0), (0, 0))
    xe = jnp.pad(jnp.concatenate([x_low[:, :, :2], v, x_high[:, :, :2]], axis=2), z_pad)
    fe = jnp.pad(jnp.concatenate([x_low[:, :, 2:], wrapped, x_high[:, :, 2:]], axis=2), z_pad)
    return xe, fe


def full_pad(xe, fe):
    wide_y = xe.shape[-1]
    return jnp.concatenate([fe[..., wide_y - 2 :], xe, fe[..., :2]], axis=-1)


def window(array_in, move_z, move_x, move_y):
    size_z = array_in.shape[-3] - 4
    size_x = array_in.shape[-2] - 4
    size_y = array_in.shape[-1] - 4
    return array_in[
        ...,
        2 + move_z : 2 + move_z + size_z,
        2 + move_x : 2 + move_x + size_x,
        2 + move_y : 2 + move_y + size_y,
    ]


def placement(starts, slots, wide):
    source = lax.broadcasted_iota(jnp.int32, (slots, wide, 2 * wide), 1)
    target = lax.broadcasted_iota(jnp.int32, (slots, wide, 2 * wide), 2)
    return (target == source + starts.astype(jnp.int32)[:, None, None]).astype(jnp.float32)


def blend_home(patches, patch_wx, patch_wy, offset_x, offset_y, live_count):
    slots, depth_z, wide_x, wide_y = patches.shape
    slot_ids = lax.broadcasted_iota(jnp.int32, (slots,), 0)
    live = (slot_ids < live_count[0, 0]).astype(jnp.float32)
    place_x = placement(offset_x[:, 0, 0], slots, wide_x)
    place_y = placement(offset_y[:, 0, 0], slots, wide_y)
    along_x = patch_wx[:, 0, :].astype(jnp.float32) * live[:, None]
    along_y = patch_wy[:, 0, :].astype(jnp.float32)
    scaled = patches.astype(jnp.float32) * along_x[:, None, :, None] * along_y[:, None, None, :]
    wide_rows = jnp.einsum("szxy,syY->szxY", scaled, place_y, precision=EXACT)
    weighted = jnp.einsum("szxY,sxX->zXY", wide_rows, place_x, precision=EXACT)
    row_weight = jnp.einsum("sx,sxX->sX", along_x, place_x, precision=EXACT)
    col_weight = jnp.einsum("sy,syY->sY", along_y, place_y, precision=EXACT)
    weight_sum = jnp.einsum("sX,sY->XY", row_weight, col_weight, precision=EXACT)
    return (weighted, weight_sum)


def relax_kernel(xe_ref, fe_ref, mc_ref, bc_ref, rate_ref, force_ref, out_ref):
    depth = out_ref.shape[1]
    wide_x = out_ref.shape[2]
    wide_y = out_ref.shape[3]
    lane = lax.broadcasted_iota(jnp.int32, (HALF, wide_y), 1)
    inside = {dy: (lane + dy >= 0) & (lane + dy < wide_y) for dy in (-2, -1, 1, 2)}

    def body(z, carry):
        for half in range(wide_x // HALF):
            rows = pl.ds(half * HALF, HALF)
            rate = rate_ref[z, rows, :]
            for comp in range(3):
                cache = {}

                def val(c, dz, dx, dy):
                    key = (c, dz, dx, dy)
                    if key not in cache:
                        span = pl.ds(2 + dx + half * HALF, HALF)
                        got = xe_ref[c, z + 2 + dz, span, :]
                        if dy != 0:
                            ring = fe_ref[c, z + 2 + dz, span, :]
                            turn = (-dy) % wide_y
                            got = jnp.where(
                                inside[dy], pltpu.roll(got, turn, 1), pltpu.roll(ring, turn, 1)
                            )
                        cache[key] = got
                    return cache[key]

                centre = val(comp, 0, 0, 0)
                laplace = 0.0
                for dim in range(3):
                    ahead = STEPS_UNIT[dim]
                    behind = tuple(-t for t in ahead)
                    laplace = laplace + mc_ref[2 * dim, z, rows, :] * (val(comp, *ahead) - centre)
                    laplace = laplace - mc_ref[2 * dim + 1, z, rows, :] * (
                        centre - val(comp, *behind)
                    )
                step = STEPS_UNIT[comp]

                def divergence(sign):
                    result = 0.0
                    for dim in range(3):
                        unit = STEPS_UNIT[dim]
                        fwd = tuple(sign * step[k] + unit[k] for k in range(3))
                        bwd = tuple(sign * step[k] - unit[k] for k in range(3))
                        result = result + 0.5 * (val(dim, *fwd) - val(dim, *bwd))
                    return result

                grad_div = 0.5 * (
                    bc_ref[2 * comp, z, rows, :] * divergence(1)
                    - bc_ref[2 * comp + 1, z, rows, :] * divergence(-1)
                )
                out_ref[comp, z, rows, :] = centre + rate * (
                    laplace + grad_div + force_ref[comp, z, rows, :]
                )
        return carry

    lax.fori_loop(0, depth, body, 0)


def relax_call(xe, fe, mc, bc, rate, forcing):
    out_shape = jax.ShapeDtypeStruct(forcing.shape, jnp.float32)
    moved = sum(a.size * a.dtype.itemsize for a in (xe, fe, mc, bc, rate, forcing)) + forcing.size * 4
    return pl.pallas_call(
        relax_kernel,
        out_shape=out_shape,
        compiler_params=pltpu.CompilerParams(vmem_limit_bytes=48 * 1024 * 1024),
        cost_estimate=pl.CostEstimate(
            flops=forcing.size * 70, transcendentals=0, bytes_accessed=moved
        ),
    )(xe, fe, mc, bc, rate, forcing)


def per_device(
    patches,
    patch_wx,
    patch_wy,
    offset_x,
    offset_y,
    block_counts,
    template,
    stiff_mu,
    stiff_lam,
    start_field,
):
    wide_x = patches.shape[2]
    wide_y = patches.shape[3]
    canvas, canvas_weight = blend_home(patches, patch_wx, patch_wy, offset_x, offset_y, block_counts)

    def quarter(upper_x, upper_y):
        cut_x = slice(upper_x * wide_x, (upper_x + 1) * wide_x)
        cut_y = slice(upper_y * wide_y, (upper_y + 1) * wide_y)
        return jnp.concatenate([canvas[:, cut_x, cut_y], canvas_weight[None, cut_x, cut_y]], axis=0)

    from_y = shifted_in(quarter(0, 1), "gy", 1)
    from_x = shifted_in(quarter(1, 0), "gx", 1)
    from_xy = diagonal_in(quarter(1, 1))
    total = quarter(0, 0) + from_y + from_x + from_xy
    weighted = total[:-1]
    weight_sum = total[-1]
    joined = (weighted / jnp.maximum(weight_sum, 1.0)[None]).astype(jnp.bfloat16)

    bulk = stiff_lam + stiff_mu
    rate = RELAX_FACTOR / (6.0 * stiff_mu + 3.0 * bulk)
    moduli = full_pad(*halo(jnp.stack([stiff_mu, bulk])))
    shear = moduli[0]
    bulk_pad = moduli[1]
    shear_here = window(shear, 0, 0, 0)
    mean_shear = []
    bulk_beside = []
    for dim in range(3):
        ahead = STEPS_UNIT[dim]
        behind = tuple(-t for t in ahead)
        mean_shear.append(0.5 * (shear_here + window(shear, *ahead)))
        mean_shear.append(0.5 * (shear_here + window(shear, *behind)))
        bulk_beside.append(window(bulk_pad, *ahead))
        bulk_beside.append(window(bulk_pad, *behind))
    mean_shear = jnp.stack(mean_shear)
    bulk_beside = jnp.stack(bulk_beside)

    image = full_pad(*halo(joined[None]))[0].astype(jnp.float32)
    centre = window(image, 0, 0, 0)
    mismatch = template.astype(jnp.float32) - centre
    slopes = []
    for dim in range(3):
        ahead = STEPS_UNIT[dim]
        behind = tuple(-t for t in ahead)
        slopes.append(0.5 * (window(image, *ahead) - window(image, *behind)) * mismatch)
    forcing = jnp.stack(slopes)

    field = start_field
    for pass_idx in range(PASSES):
        xe, fe = halo(field)
        field = relax_call(xe, fe, mean_shear, bulk_beside, rate, forcing)
    return (joined, field)


def solution(mesh):
    placed = (
        P(None, None, "gx", "gy"),
        P(None, "gy", "gx"),
        P(None, "gx", "gy"),
        P(None, "gx", "gy"),
        P(None, "gx", "gy"),
        P("gx", "gy"),
        P(None, "gx", "gy"),
        P(None, "gx", "gy"),
        P(None, "gx", "gy"),
        P(None, None, "gx", "gy"),
    )
    return jax.shard_map(
        per_device,
        mesh=mesh,
        in_specs=placed,
        out_specs=(P(None, "gx", "gy"), P(None, None, "gx", "gy")),
        check_vma=False,
    )
```

```python
import jax
import jax.numpy as jnp
from jax import lax
from jax.experimental import pallas as pl
from jax.experimental.pallas import tpu as pltpu
from jax.sharding import PartitionSpec as P

PASSES = 4


RELAX_FACTOR = 0.9
STEPS_UNIT = ((1, 0, 0), (0, 1, 0), (0, 0, 1))
EXACT = lax.Precision.HIGHEST
HALF = 8


def shifted_in(block, axis, distance):
    count = lax.axis_size(axis)
    route = [(i, i + distance) for i in range(count) if 0 <= i + distance < count]
    return lax.ppermute(block, axis, route)


def diagonal_in(block):
    nx = lax.axis_size("gx")
    ny = lax.axis_size("gy")
    route = [(i * ny + j, (i + 1) * ny + j + 1) for i in range(nx - 1) for j in range(ny - 1)]
    return lax.ppermute(block, ("gx", "gy"), route)


def edge_lanes(wide_y):
    lanes = jnp.array([0, 1, wide_y - 2, wide_y - 1], jnp.int32)
    return (lax.broadcasted_iota(jnp.int32, (4, wide_y), 1) == lanes[:, None]).astype(jnp.float32)


def halo(v):
    chans, depth, wide_x, wide_y = v.shape
    pick = edge_lanes(wide_y)
    rows = v.reshape(chans * depth * wide_x, wide_y)
    strips = jnp.einsum("ky,ry->kr", pick, rows, precision=EXACT)
    y_high = shifted_in(strips[:2], "gy", -1)
    y_low = shifted_in(strips[2:], "gy", 1)
    arrived = jnp.concatenate([y_high, y_low], axis=0)
    wrapped = jnp.einsum("kr,ky->ry", arrived, pick, precision=EXACT).reshape(v.shape)
    upward = jnp.concatenate([v[:, :, wide_x - 2 :], wrapped[:, :, wide_x - 2 :]], axis=2)
    downward = jnp.concatenate([v[:, :, :2], wrapped[:, :, :2]], axis=2)
    x_low = shifted_in(upward, "gx", 1)
    x_high = shifted_in(downward, "gx", -1)
    z_pad = ((0, 0), (2, 2), (0, 0), (0, 0))
    xe = jnp.pad(jnp.concatenate([x_low[:, :, :2], v, x_high[:, :, :2]], axis=2), z_pad)
    fe = jnp.pad(jnp.concatenate([x_low[:, :, 2:], wrapped, x_high[:, :, 2:]], axis=2), z_pad)
    return xe, fe


def full_pad(xe, fe):
    wide_y = xe.shape[-1]
    return jnp.concatenate([fe[..., wide_y - 2 :], xe, fe[..., :2]], axis=-1)


def window(array_in, move_z, move_x, move_y):
    size_z = array_in.shape[-3] - 4
    size_x = array_in.shape[-2] - 4
    size_y = array_in.shape[-1] - 4
    return array_in[
        ...,
        2 + move_z : 2 + move_z + size_z,
        2 + move_x : 2 + move_x + size_x,
        2 + move_y : 2 + move_y + size_y,
    ]


def placement(starts, slots, wide):
    source = lax.broadcasted_iota(jnp.int32, (slots, wide, 2 * wide), 1)
    target = lax.broadcasted_iota(jnp.int32, (slots, wide, 2 * wide), 2)
    return (target == source + starts.astype(jnp.int32)[:, None, None]).astype(jnp.float32)


def blend_home(patches, patch_wx, patch_wy, offset_x, offset_y, live_count):
    slots, depth_z, wide_x, wide_y = patches.shape
    slot_ids = lax.broadcasted_iota(jnp.int32, (slots,), 0)
    live = (slot_ids < live_count[0, 0]).astype(jnp.float32)
    place_x = placement(offset_x[:, 0, 0], slots, wide_x)
    place_y = placement(offset_y[:, 0, 0], slots, wide_y)
    along_x = patch_wx[:, 0, :].astype(jnp.float32) * live[:, None]
    along_y = patch_wy[:, 0, :].astype(jnp.float32)
    scaled = patches.astype(jnp.float32) * along_x[:, None, :, None] * along_y[:, None, None, :]
    wide_rows = jnp.einsum("szxy,syY->szxY", scaled, place_y, precision=EXACT)
    weighted = jnp.einsum("szxY,sxX->zXY", wide_rows, place_x, precision=EXACT)
    row_weight = jnp.einsum("sx,sxX->sX", along_x, place_x, precision=EXACT)
    col_weight = jnp.einsum("sy,syY->sY", along_y, place_y, precision=EXACT)
    weight_sum = jnp.einsum("sX,sY->XY", row_weight, col_weight, precision=EXACT)
    return (weighted, weight_sum)


def relax_kernel(xe_ref, fe_ref, mc_ref, bc_ref, rate_ref, force_ref, out_ref):
    chunk = out_ref.shape[1]
    wide_x = out_ref.shape[2]
    wide_y = out_ref.shape[3]
    first = pl.program_id(0) * chunk
    lane = lax.broadcasted_iota(jnp.int32, (HALF, wide_y), 1)
    inside = {dy: (lane + dy >= 0) & (lane + dy < wide_y) for dy in (-2, -1, 1, 2)}

    def body(z, carry):
        plane = first + z + 2
        for half in range(wide_x // HALF):
            rows = pl.ds(half * HALF, HALF)
            rate = rate_ref[z, rows, :]
            for comp in range(3):
                cache = {}

                def val(c, dz, dx, dy):
                    key = (c, dz, dx, dy)
                    if key not in cache:
                        span = pl.ds(2 + dx + half * HALF, HALF)
                        got = xe_ref[c, plane + dz, span, :]
                        if dy != 0:
                            ring = fe_ref[c, plane + dz, span, :]
                            turn = (-dy) % wide_y
                            got = jnp.where(
                                inside[dy], pltpu.roll(got, turn, 1), pltpu.roll(ring, turn, 1)
                            )
                        cache[key] = got
                    return cache[key]

                centre = val(comp, 0, 0, 0)
                laplace = 0.0
                for dim in range(3):
                    ahead = STEPS_UNIT[dim]
                    behind = tuple(-t for t in ahead)
                    laplace = laplace + mc_ref[2 * dim, z, rows, :] * (val(comp, *ahead) - centre)
                    laplace = laplace - mc_ref[2 * dim + 1, z, rows, :] * (
                        centre - val(comp, *behind)
                    )
                step = STEPS_UNIT[comp]

                def divergence(sign):
                    result = 0.0
                    for dim in range(3):
                        unit = STEPS_UNIT[dim]
                        fwd = tuple(sign * step[k] + unit[k] for k in range(3))
                        bwd = tuple(sign * step[k] - unit[k] for k in range(3))
                        result = result + 0.5 * (val(dim, *fwd) - val(dim, *bwd))
                    return result

                grad_div = 0.5 * (
                    bc_ref[2 * comp, z, rows, :] * divergence(1)
                    - bc_ref[2 * comp + 1, z, rows, :] * divergence(-1)
                )
                out_ref[comp, z, rows, :] = centre + rate * (
                    laplace + grad_div + force_ref[comp, z, rows, :]
                )
        return carry

    lax.fori_loop(0, chunk, body, 0)


def relax_call(xe, fe, mc, bc, rate, forcing, chunk=8):
    chans, depth, wide_x, wide_y = forcing.shape
    out_shape = jax.ShapeDtypeStruct(forcing.shape, jnp.float32)
    moved = sum(a.size * a.dtype.itemsize for a in (xe, fe, mc, bc, rate, forcing)) + forcing.size * 4
    whole = pl.BlockSpec(xe.shape, lambda g: (0, 0, 0, 0))
    six = pl.BlockSpec((mc.shape[0], chunk, wide_x, wide_y), lambda g: (0, g, 0, 0))
    three = pl.BlockSpec((chans, chunk, wide_x, wide_y), lambda g: (0, g, 0, 0))
    one = pl.BlockSpec((chunk, wide_x, wide_y), lambda g: (g, 0, 0))
    return pl.pallas_call(
        relax_kernel,
        out_shape=out_shape,
        grid=(depth // chunk,),
        in_specs=[whole, whole, six, six, one, three],
        out_specs=three,
        compiler_params=pltpu.CompilerParams(vmem_limit_bytes=48 * 1024 * 1024),
        cost_estimate=pl.CostEstimate(
            flops=forcing.size * 70, transcendentals=0, bytes_accessed=moved
        ),
    )(xe, fe, mc, bc, rate, forcing)


def per_device(
    patches,
    patch_wx,
    patch_wy,
    offset_x,
    offset_y,
    block_counts,
    template,
    stiff_mu,
    stiff_lam,
    start_field,
):
    wide_x = patches.shape[2]
    wide_y = patches.shape[3]
    canvas, canvas_weight = blend_home(patches, patch_wx, patch_wy, offset_x, offset_y, block_counts)

    def quarter(upper_x, upper_y):
        cut_x = slice(upper_x * wide_x, (upper_x + 1) * wide_x)
        cut_y = slice(upper_y * wide_y, (upper_y + 1) * wide_y)
        return jnp.concatenate([canvas[:, cut_x, cut_y], canvas_weight[None, cut_x, cut_y]], axis=0)

    from_y = shifted_in(quarter(0, 1), "gy", 1)
    from_x = shifted_in(quarter(1, 0), "gx", 1)
    from_xy = diagonal_in(quarter(1, 1))
    total = quarter(0, 0) + from_y + from_x + from_xy
    weighted = total[:-1]
    weight_sum = total[-1]
    joined = (weighted / jnp.maximum(weight_sum, 1.0)[None]).astype(jnp.bfloat16)

    bulk = stiff_lam + stiff_mu
    rate = RELAX_FACTOR / (6.0 * stiff_mu + 3.0 * bulk)
    moduli = full_pad(*halo(jnp.stack([stiff_mu, bulk])))
    shear = moduli[0]
    bulk_pad = moduli[1]
    shear_here = window(shear, 0, 0, 0)
    mean_shear = []
    bulk_beside = []
    for dim in range(3):
        ahead = STEPS_UNIT[dim]
        behind = tuple(-t for t in ahead)
        mean_shear.append(0.5 * (shear_here + window(shear, *ahead)))
        mean_shear.append(0.5 * (shear_here + window(shear, *behind)))
        bulk_beside.append(window(bulk_pad, *ahead))
        bulk_beside.append(window(bulk_pad, *behind))
    mean_shear = jnp.stack(mean_shear)
    bulk_beside = jnp.stack(bulk_beside)

    image = full_pad(*halo(joined[None].astype(jnp.float32)))[0]
    centre = window(image, 0, 0, 0)
    mismatch = template.astype(jnp.float32) - centre
    slopes = []
    for dim in range(3):
        ahead = STEPS_UNIT[dim]
        behind = tuple(-t for t in ahead)
        slopes.append(0.5 * (window(image, *ahead) - window(image, *behind)) * mismatch)
    forcing = jnp.stack(slopes)

    def one_pass(pass_idx, field):
        xe, fe = halo(field)
        return relax_call(xe, fe, mean_shear, bulk_beside, rate, forcing)

    field = lax.fori_loop(0, PASSES, one_pass, start_field)
    return (joined, field)


def solution(mesh):
    placed = (
        P(None, None, "gx", "gy"),
        P(None, "gy", "gx"),
        P(None, "gx", "gy"),
        P(None, "gx", "gy"),
        P(None, "gx", "gy"),
        P("gx", "gy"),
        P(None, "gx", "gy"),
        P(None, "gx", "gy"),
        P(None, "gx", "gy"),
        P(None, None, "gx", "gy"),
    )
    return jax.shard_map(
        per_device,
        mesh=mesh,
        in_specs=placed,
        out_specs=(P(None, "gx", "gy"), P(None, None, "gx", "gy")),
        check_vma=False,
    )
```

```python
import jax
import jax.numpy as jnp
from jax import lax
from jax.experimental import pallas as pl
from jax.experimental.pallas import tpu as pltpu
from jax.sharding import PartitionSpec as P

PASSES = 4


RELAX_FACTOR = 0.9
STEPS_UNIT = ((1, 0, 0), (0, 1, 0), (0, 0, 1))
EXACT = lax.Precision.HIGHEST
HALF = 8


def shifted_in(block, axis, distance):
    count = lax.axis_size(axis)
    route = [(i, i + distance) for i in range(count) if 0 <= i + distance < count]
    return lax.ppermute(block, axis, route)


def diagonal_in(block):
    nx = lax.axis_size("gx")
    ny = lax.axis_size("gy")
    route = [(i * ny + j, (i + 1) * ny + j + 1) for i in range(nx - 1) for j in range(ny - 1)]
    return lax.ppermute(block, ("gx", "gy"), route)


def edge_lanes(wide_y):
    lanes = jnp.array([0, 1, wide_y - 2, wide_y - 1], jnp.int32)
    return (lax.broadcasted_iota(jnp.int32, (4, wide_y), 1) == lanes[:, None]).astype(jnp.float32)


def exact_pick(equation, values, pick):
    high = lax.reduce_precision(values, exponent_bits=8, mantissa_bits=7)
    rest = values - high
    middle = lax.reduce_precision(rest, exponent_bits=8, mantissa_bits=7)
    low = rest - middle
    ones = pick.astype(jnp.bfloat16)

    def part(piece):
        return jnp.einsum(
            equation, ones, piece.astype(jnp.bfloat16), preferred_element_type=jnp.float32
        )

    return (part(high) + part(middle)) + part(low)


def halo(v):
    chans, depth, wide_x, wide_y = v.shape
    pick = edge_lanes(wide_y)
    rows = v.reshape(chans * depth * wide_x, wide_y)
    strips = exact_pick("ky,ry->kr", rows, pick).reshape(4, chans, depth, wide_x)
    first = strips[:2]
    last = strips[2:]
    nx = lax.axis_size("gx")
    ny = lax.axis_size("gy")

    def corner(block, step_x, step_y):
        route = []
        for i in range(nx):
            for j in range(ny):
                if 0 <= i + step_x < nx and 0 <= j + step_y < ny:
                    route.append((i * ny + j, (i + step_x) * ny + j + step_y))
        return lax.ppermute(block, ("gx", "gy"), route)

    y_high = shifted_in(first, "gy", -1)
    y_low = shifted_in(last, "gy", 1)
    x_low = shifted_in(v[:, :, wide_x - 2 :], "gx", 1)
    x_high = shifted_in(v[:, :, :2], "gx", -1)
    low_high = corner(first[..., wide_x - 2 :], 1, -1)
    low_low = corner(last[..., wide_x - 2 :], 1, 1)
    high_high = corner(first[..., :2], -1, -1)
    high_low = corner(last[..., :2], -1, 1)
    arrived = jnp.concatenate(
        [
            jnp.concatenate([low_high, y_high, high_high], axis=-1),
            jnp.concatenate([low_low, y_low, high_low], axis=-1),
        ],
        axis=0,
    )
    tall = wide_x + 4
    wrapped = exact_pick("ky,kr->ry", arrived.reshape(4, chans * depth * tall), pick)
    z_pad = ((0, 0), (2, 2), (0, 0), (0, 0))
    xe = jnp.pad(jnp.concatenate([x_low, v, x_high], axis=2), z_pad)
    fe = jnp.pad(wrapped.reshape(chans, depth, tall, wide_y), z_pad)
    return xe, fe


def full_pad(xe, fe):
    wide_y = xe.shape[-1]
    return jnp.concatenate([fe[..., wide_y - 2 :], xe, fe[..., :2]], axis=-1)


def window(array_in, move_z, move_x, move_y):
    size_z = array_in.shape[-3] - 4
    size_x = array_in.shape[-2] - 4
    size_y = array_in.shape[-1] - 4
    return array_in[
        ...,
        2 + move_z : 2 + move_z + size_z,
        2 + move_x : 2 + move_x + size_x,
        2 + move_y : 2 + move_y + size_y,
    ]


def placement(starts, slots, wide):
    source = lax.broadcasted_iota(jnp.int32, (slots, wide, 2 * wide), 1)
    target = lax.broadcasted_iota(jnp.int32, (slots, wide, 2 * wide), 2)
    return (target == source + starts.astype(jnp.int32)[:, None, None]).astype(jnp.float32)


def blend_home(patches, patch_wx, patch_wy, offset_x, offset_y, live_count):
    slots, depth_z, wide_x, wide_y = patches.shape
    slot_ids = lax.broadcasted_iota(jnp.int32, (slots,), 0)
    live = (slot_ids < live_count[0, 0]).astype(jnp.float32)
    place_x = placement(offset_x[:, 0, 0], slots, wide_x)
    place_y = placement(offset_y[:, 0, 0], slots, wide_y)
    along_x = patch_wx[:, 0, :].astype(jnp.float32) * live[:, None]
    along_y = patch_wy[:, 0, :].astype(jnp.float32)
    scaled = patches.astype(jnp.float32) * along_x[:, None, :, None] * along_y[:, None, None, :]
    wide_rows = jnp.einsum("szxy,syY->szxY", scaled, place_y, precision=EXACT)
    weighted = jnp.einsum("szxY,sxX->zXY", wide_rows, place_x, precision=EXACT)
    row_weight = jnp.einsum("sx,sxX->sX", along_x, place_x, precision=EXACT)
    col_weight = jnp.einsum("sy,syY->sY", along_y, place_y, precision=EXACT)
    weight_sum = jnp.einsum("sX,sY->XY", row_weight, col_weight, precision=EXACT)
    return (weighted, weight_sum)


def relax_kernel(xe_ref, fe_ref, mc_ref, bc_ref, rate_ref, force_ref, out_ref):
    chunk = out_ref.shape[1]
    wide_x = out_ref.shape[2]
    wide_y = out_ref.shape[3]
    first = pl.program_id(0) * chunk
    lane = lax.broadcasted_iota(jnp.int32, (HALF, wide_y), 1)
    inside = {dy: (lane + dy >= 0) & (lane + dy < wide_y) for dy in (-2, -1, 1, 2)}

    def body(z, carry):
        plane = first + z + 2
        for half in range(wide_x // HALF):
            rows = pl.ds(half * HALF, HALF)
            rate = rate_ref[z, rows, :]
            for comp in range(3):
                cache = {}

                def val(c, dz, dx, dy):
                    key = (c, dz, dx, dy)
                    if key not in cache:
                        span = pl.ds(2 + dx + half * HALF, HALF)
                        got = xe_ref[c, plane + dz, span, :]
                        if dy != 0:
                            ring = fe_ref[c, plane + dz, span, :]
                            turn = (-dy) % wide_y
                            got = jnp.where(
                                inside[dy], pltpu.roll(got, turn, 1), pltpu.roll(ring, turn, 1)
                            )
                        cache[key] = got
                    return cache[key]

                centre = val(comp, 0, 0, 0)
                laplace = 0.0
                for dim in range(3):
                    ahead = STEPS_UNIT[dim]
                    behind = tuple(-t for t in ahead)
                    laplace = laplace + mc_ref[2 * dim, z, rows, :] * (val(comp, *ahead) - centre)
                    laplace = laplace - mc_ref[2 * dim + 1, z, rows, :] * (
                        centre - val(comp, *behind)
                    )
                step = STEPS_UNIT[comp]

                def divergence(sign):
                    result = 0.0
                    for dim in range(3):
                        unit = STEPS_UNIT[dim]
                        fwd = tuple(sign * step[k] + unit[k] for k in range(3))
                        bwd = tuple(sign * step[k] - unit[k] for k in range(3))
                        result = result + 0.5 * (val(dim, *fwd) - val(dim, *bwd))
                    return result

                grad_div = 0.5 * (
                    bc_ref[2 * comp, z, rows, :] * divergence(1)
                    - bc_ref[2 * comp + 1, z, rows, :] * divergence(-1)
                )
                out_ref[comp, z, rows, :] = centre + rate * (
                    laplace + grad_div + force_ref[comp, z, rows, :]
                )
        return carry

    lax.fori_loop(0, chunk, body, 0)


def relax_call(xe, fe, mc, bc, rate, forcing, chunk=8):
    chans, depth, wide_x, wide_y = forcing.shape
    out_shape = jax.ShapeDtypeStruct(forcing.shape, jnp.float32)
    moved = sum(a.size * a.dtype.itemsize for a in (xe, fe, mc, bc, rate, forcing)) + forcing.size * 4
    whole = pl.BlockSpec(xe.shape, lambda g: (0, 0, 0, 0))
    six = pl.BlockSpec((mc.shape[0], chunk, wide_x, wide_y), lambda g: (0, g, 0, 0))
    three = pl.BlockSpec((chans, chunk, wide_x, wide_y), lambda g: (0, g, 0, 0))
    one = pl.BlockSpec((chunk, wide_x, wide_y), lambda g: (g, 0, 0))
    return pl.pallas_call(
        relax_kernel,
        out_shape=out_shape,
        grid=(depth // chunk,),
        in_specs=[whole, whole, six, six, one, three],
        out_specs=three,
        compiler_params=pltpu.CompilerParams(vmem_limit_bytes=48 * 1024 * 1024),
        cost_estimate=pl.CostEstimate(
            flops=forcing.size * 70, transcendentals=0, bytes_accessed=moved
        ),
    )(xe, fe, mc, bc, rate, forcing)


def per_device(
    patches,
    patch_wx,
    patch_wy,
    offset_x,
    offset_y,
    block_counts,
    template,
    stiff_mu,
    stiff_lam,
    start_field,
):
    wide_x = patches.shape[2]
    wide_y = patches.shape[3]
    canvas, canvas_weight = blend_home(patches, patch_wx, patch_wy, offset_x, offset_y, block_counts)

    def quarter(upper_x, upper_y):
        cut_x = slice(upper_x * wide_x, (upper_x + 1) * wide_x)
        cut_y = slice(upper_y * wide_y, (upper_y + 1) * wide_y)
        return jnp.concatenate([canvas[:, cut_x, cut_y], canvas_weight[None, cut_x, cut_y]], axis=0)

    from_y = shifted_in(quarter(0, 1), "gy", 1)
    from_x = shifted_in(quarter(1, 0), "gx", 1)
    from_xy = diagonal_in(quarter(1, 1))
    total = quarter(0, 0) + from_y + from_x + from_xy
    weighted = total[:-1]
    weight_sum = total[-1]
    joined = (weighted / jnp.maximum(weight_sum, 1.0)[None]).astype(jnp.bfloat16)

    bulk = stiff_lam + stiff_mu
    rate = RELAX_FACTOR / (6.0 * stiff_mu + 3.0 * bulk)
    moduli = full_pad(*halo(jnp.stack([stiff_mu, bulk])))
    shear = moduli[0]
    bulk_pad = moduli[1]
    shear_here = window(shear, 0, 0, 0)
    mean_shear = []
    bulk_beside = []
    for dim in range(3):
        ahead = STEPS_UNIT[dim]
        behind = tuple(-t for t in ahead)
        mean_shear.append(0.5 * (shear_here + window(shear, *ahead)))
        mean_shear.append(0.5 * (shear_here + window(shear, *behind)))
        bulk_beside.append(window(bulk_pad, *ahead))
        bulk_beside.append(window(bulk_pad, *behind))
    mean_shear = jnp.stack(mean_shear)
    bulk_beside = jnp.stack(bulk_beside)

    image = full_pad(*halo(joined[None].astype(jnp.float32)))[0]
    centre = window(image, 0, 0, 0)
    mismatch = template.astype(jnp.float32) - centre
    slopes = []
    for dim in range(3):
        ahead = STEPS_UNIT[dim]
        behind = tuple(-t for t in ahead)
        slopes.append(0.5 * (window(image, *ahead) - window(image, *behind)) * mismatch)
    forcing = jnp.stack(slopes)

    def one_pass(pass_idx, field):
        xe, fe = halo(field)
        return relax_call(xe, fe, mean_shear, bulk_beside, rate, forcing)

    field = lax.fori_loop(0, PASSES, one_pass, start_field)
    return (joined, field)


def solution(mesh):
    placed = (
        P(None, None, "gx", "gy"),
        P(None, "gy", "gx"),
        P(None, "gx", "gy"),
        P(None, "gx", "gy"),
        P(None, "gx", "gy"),
        P("gx", "gy"),
        P(None, "gx", "gy"),
        P(None, "gx", "gy"),
        P(None, "gx", "gy"),
        P(None, None, "gx", "gy"),
    )
    return jax.shard_map(
        per_device,
        mesh=mesh,
        in_specs=placed,
        out_specs=(P(None, "gx", "gy"), P(None, None, "gx", "gy")),
        check_vma=False,
    )
```

```python
import jax
import jax.numpy as jnp
from jax import lax
from jax.experimental import pallas as pl
from jax.experimental.pallas import tpu as pltpu
from jax.sharding import PartitionSpec as P

PASSES = 4


RELAX_FACTOR = 0.9
STEPS_UNIT = ((1, 0, 0), (0, 1, 0), (0, 0, 1))
EXACT = lax.Precision.HIGHEST
HALF = 8


def shifted_in(block, axis, distance):
    count = lax.axis_size(axis)
    route = [(i, i + distance) for i in range(count) if 0 <= i + distance < count]
    return lax.ppermute(block, axis, route)


def diagonal_in(block):
    nx = lax.axis_size("gx")
    ny = lax.axis_size("gy")
    route = [(i * ny + j, (i + 1) * ny + j + 1) for i in range(nx - 1) for j in range(ny - 1)]
    return lax.ppermute(block, ("gx", "gy"), route)


def edge_lanes(wide_y):
    lanes = jnp.array([0, 1, wide_y - 2, wide_y - 1], jnp.int32)
    return (lax.broadcasted_iota(jnp.int32, (4, wide_y), 1) == lanes[:, None]).astype(jnp.float32)


def halo(v):
    chans, depth, wide_x, wide_y = v.shape
    pick = edge_lanes(wide_y)
    rows = v.reshape(chans * depth * wide_x, wide_y)
    strips = jnp.einsum("ky,ry->kr", pick, rows, precision=EXACT)
    y_high = shifted_in(strips[:2], "gy", -1)
    y_low = shifted_in(strips[2:], "gy", 1)
    arrived = jnp.concatenate([y_high, y_low], axis=0)
    wrapped = jnp.einsum("kr,ky->ry", arrived, pick, precision=EXACT).reshape(v.shape)
    upward = jnp.concatenate([v[:, :, wide_x - 2 :], wrapped[:, :, wide_x - 2 :]], axis=2)
    downward = jnp.concatenate([v[:, :, :2], wrapped[:, :, :2]], axis=2)
    x_low = shifted_in(upward, "gx", 1)
    x_high = shifted_in(downward, "gx", -1)
    z_pad = ((0, 0), (2, 2), (0, 0), (0, 0))
    xe = jnp.pad(jnp.concatenate([x_low[:, :, :2], v, x_high[:, :, :2]], axis=2), z_pad)
    fe = jnp.pad(jnp.concatenate([x_low[:, :, 2:], wrapped, x_high[:, :, 2:]], axis=2), z_pad)
    return xe, fe


def full_pad(xe, fe):
    wide_y = xe.shape[-1]
    return jnp.concatenate([fe[..., wide_y - 2 :], xe, fe[..., :2]], axis=-1)


def window(array_in, move_z, move_x, move_y):
    size_z = array_in.shape[-3] - 4
    size_x = array_in.shape[-2] - 4
    size_y = array_in.shape[-1] - 4
    return array_in[
        ...,
        2 + move_z : 2 + move_z + size_z,
        2 + move_x : 2 + move_x + size_x,
        2 + move_y : 2 + move_y + size_y,
    ]


def placement(starts, slots, wide):
    source = lax.broadcasted_iota(jnp.int32, (slots, wide, 2 * wide), 1)
    target = lax.broadcasted_iota(jnp.int32, (slots, wide, 2 * wide), 2)
    return (target == source + starts.astype(jnp.int32)[:, None, None]).astype(jnp.float32)


def blend_home(patches, patch_wx, patch_wy, offset_x, offset_y, live_count):
    slots, depth_z, wide_x, wide_y = patches.shape
    slot_ids = lax.broadcasted_iota(jnp.int32, (slots,), 0)
    live = (slot_ids < live_count[0, 0]).astype(jnp.float32)
    place_x = placement(offset_x[:, 0, 0], slots, wide_x)
    place_y = placement(offset_y[:, 0, 0], slots, wide_y)
    along_x = patch_wx[:, 0, :].astype(jnp.float32) * live[:, None]
    along_y = patch_wy[:, 0, :].astype(jnp.float32)
    scaled = patches.astype(jnp.float32) * along_x[:, None, :, None] * along_y[:, None, None, :]
    wide_rows = jnp.einsum("szxy,syY->szxY", scaled, place_y, precision=EXACT)
    weighted = jnp.einsum("szxY,sxX->zXY", wide_rows, place_x, precision=EXACT)
    row_weight = jnp.einsum("sx,sxX->sX", along_x, place_x, precision=EXACT)
    col_weight = jnp.einsum("sy,syY->sY", along_y, place_y, precision=EXACT)
    weight_sum = jnp.einsum("sX,sY->XY", row_weight, col_weight, precision=EXACT)
    return (weighted, weight_sum)


def relax_kernel(xe_ref, fe_ref, mc_ref, bc_ref, rate_ref, force_ref, out_ref):
    chunk = out_ref.shape[1]
    wide_x = out_ref.shape[2]
    wide_y = out_ref.shape[3]
    first = pl.program_id(0) * chunk
    lane = lax.broadcasted_iota(jnp.int32, (HALF, wide_y), 1)
    inside = {dy: (lane + dy >= 0) & (lane + dy < wide_y) for dy in (-2, -1, 1, 2)}

    def body(z, carry):
        plane = first + z + 2
        for half in range(wide_x // HALF):
            rows = pl.ds(half * HALF, HALF)
            rate = rate_ref[z, rows, :]
            for comp in range(3):
                cache = {}

                def val(c, dz, dx, dy):
                    key = (c, dz, dx, dy)
                    if key not in cache:
                        span = pl.ds(2 + dx + half * HALF, HALF)
                        got = xe_ref[c, plane + dz, span, :]
                        if dy != 0:
                            ring = fe_ref[c, plane + dz, span, :]
                            turn = (-dy) % wide_y
                            got = jnp.where(
                                inside[dy], pltpu.roll(got, turn, 1), pltpu.roll(ring, turn, 1)
                            )
                        cache[key] = got
                    return cache[key]

                centre = val(comp, 0, 0, 0)
                laplace = 0.0
                for dim in range(3):
                    ahead = STEPS_UNIT[dim]
                    behind = tuple(-t for t in ahead)
                    laplace = laplace + mc_ref[2 * dim, z, rows, :] * (val(comp, *ahead) - centre)
                    laplace = laplace - mc_ref[2 * dim + 1, z, rows, :] * (
                        centre - val(comp, *behind)
                    )
                step = STEPS_UNIT[comp]

                def divergence(sign):
                    result = 0.0
                    for dim in range(3):
                        unit = STEPS_UNIT[dim]
                        fwd = tuple(sign * step[k] + unit[k] for k in range(3))
                        bwd = tuple(sign * step[k] - unit[k] for k in range(3))
                        result = result + 0.5 * (val(dim, *fwd) - val(dim, *bwd))
                    return result

                grad_div = 0.5 * (
                    bc_ref[2 * comp, z, rows, :] * divergence(1)
                    - bc_ref[2 * comp + 1, z, rows, :] * divergence(-1)
                )
                out_ref[comp, z, rows, :] = centre + rate * (
                    laplace + grad_div + force_ref[comp, z, rows, :]
                )
        return carry

    lax.fori_loop(0, chunk, body, 0)


def relax_call(xe, fe, mc, bc, rate, forcing, chunk=8):
    chans, depth, wide_x, wide_y = forcing.shape
    out_shape = jax.ShapeDtypeStruct(forcing.shape, jnp.float32)
    moved = sum(a.size * a.dtype.itemsize for a in (xe, fe, mc, bc, rate, forcing)) + forcing.size * 4
    whole = pl.BlockSpec(xe.shape, lambda g: (0, 0, 0, 0))
    six = pl.BlockSpec((mc.shape[0], chunk, wide_x, wide_y), lambda g: (0, g, 0, 0))
    three = pl.BlockSpec((chans, chunk, wide_x, wide_y), lambda g: (0, g, 0, 0))
    one = pl.BlockSpec((chunk, wide_x, wide_y), lambda g: (g, 0, 0))
    return pl.pallas_call(
        relax_kernel,
        out_shape=out_shape,
        grid=(depth // chunk,),
        in_specs=[whole, whole, six, six, one, three],
        out_specs=three,
        compiler_params=pltpu.CompilerParams(vmem_limit_bytes=48 * 1024 * 1024),
        cost_estimate=pl.CostEstimate(
            flops=forcing.size * 70, transcendentals=0, bytes_accessed=moved
        ),
    )(xe, fe, mc, bc, rate, forcing)


def per_device(
    patches,
    patch_wx,
    patch_wy,
    offset_x,
    offset_y,
    block_counts,
    template,
    stiff_mu,
    stiff_lam,
    start_field,
):
    wide_x = patches.shape[2]
    wide_y = patches.shape[3]
    canvas, canvas_weight = blend_home(patches, patch_wx, patch_wy, offset_x, offset_y, block_counts)

    def quarter(upper_x, upper_y):
        cut_x = slice(upper_x * wide_x, (upper_x + 1) * wide_x)
        cut_y = slice(upper_y * wide_y, (upper_y + 1) * wide_y)
        return jnp.concatenate([canvas[:, cut_x, cut_y], canvas_weight[None, cut_x, cut_y]], axis=0)

    from_y = shifted_in(quarter(0, 1), "gy", 1)
    from_x = shifted_in(quarter(1, 0), "gx", 1)
    from_xy = diagonal_in(quarter(1, 1))
    total = quarter(0, 0) + from_y + from_x + from_xy
    weighted = total[:-1]
    weight_sum = total[-1]
    joined = (weighted / jnp.maximum(weight_sum, 1.0)[None]).astype(jnp.bfloat16)

    bulk = stiff_lam + stiff_mu
    rate = RELAX_FACTOR / (6.0 * stiff_mu + 3.0 * bulk)
    padded = full_pad(*halo(jnp.stack([stiff_mu, bulk, joined.astype(jnp.float32)])))
    shear = padded[0]
    bulk_pad = padded[1]
    image = padded[2]
    shear_here = window(shear, 0, 0, 0)
    mean_shear = []
    bulk_beside = []
    for dim in range(3):
        ahead = STEPS_UNIT[dim]
        behind = tuple(-t for t in ahead)
        mean_shear.append(0.5 * (shear_here + window(shear, *ahead)))
        mean_shear.append(0.5 * (shear_here + window(shear, *behind)))
        bulk_beside.append(window(bulk_pad, *ahead))
        bulk_beside.append(window(bulk_pad, *behind))
    mean_shear = jnp.stack(mean_shear)
    bulk_beside = jnp.stack(bulk_beside)

    centre = window(image, 0, 0, 0)
    mismatch = template.astype(jnp.float32) - centre
    slopes = []
    for dim in range(3):
        ahead = STEPS_UNIT[dim]
        behind = tuple(-t for t in ahead)
        slopes.append(0.5 * (window(image, *ahead) - window(image, *behind)) * mismatch)
    forcing = jnp.stack(slopes)

    def one_pass(pass_idx, field):
        xe, fe = halo(field)
        return relax_call(xe, fe, mean_shear, bulk_beside, rate, forcing)

    field = lax.fori_loop(0, PASSES, one_pass, start_field)
    return (joined, field)


def solution(mesh):
    placed = (
        P(None, None, "gx", "gy"),
        P(None, "gy", "gx"),
        P(None, "gx", "gy"),
        P(None, "gx", "gy"),
        P(None, "gx", "gy"),
        P("gx", "gy"),
        P(None, "gx", "gy"),
        P(None, "gx", "gy"),
        P(None, "gx", "gy"),
        P(None, None, "gx", "gy"),
    )
    return jax.shard_map(
        per_device,
        mesh=mesh,
        in_specs=placed,
        out_specs=(P(None, "gx", "gy"), P(None, None, "gx", "gy")),
        check_vma=False,
    )
```

```python
import jax
import jax.numpy as jnp
from jax import lax
from jax.experimental import pallas as pl
from jax.experimental.pallas import tpu as pltpu
from jax.sharding import PartitionSpec as P

PASSES = 4


RELAX_FACTOR = 0.9
STEPS_UNIT = ((1, 0, 0), (0, 1, 0), (0, 0, 1))
EXACT = lax.Precision.HIGHEST
HALF = 8


def shifted_in(block, axis, distance):
    count = lax.axis_size(axis)
    route = [(i, i + distance) for i in range(count) if 0 <= i + distance < count]
    return lax.ppermute(block, axis, route)


def diagonal_in(block):
    nx = lax.axis_size("gx")
    ny = lax.axis_size("gy")
    route = [(i * ny + j, (i + 1) * ny + j + 1) for i in range(nx - 1) for j in range(ny - 1)]
    return lax.ppermute(block, ("gx", "gy"), route)


def edge_lanes(wide_y):
    lanes = jnp.array([0, 1, wide_y - 2, wide_y - 1], jnp.int32)
    return (lax.broadcasted_iota(jnp.int32, (4, wide_y), 1) == lanes[:, None]).astype(jnp.float32)


def halo(v):
    chans, depth, wide_x, wide_y = v.shape
    pick = edge_lanes(wide_y)
    rows = v.reshape(chans * depth * wide_x, wide_y)
    strips = jnp.einsum("ky,ry->kr", pick, rows, precision=EXACT)
    y_high = shifted_in(strips[:2], "gy", -1)
    y_low = shifted_in(strips[2:], "gy", 1)
    arrived = jnp.concatenate([y_high, y_low], axis=0)
    wrapped = jnp.einsum("kr,ky->ry", arrived, pick, precision=EXACT).reshape(v.shape)
    upward = jnp.concatenate([v[:, :, wide_x - 2 :], wrapped[:, :, wide_x - 2 :]], axis=2)
    downward = jnp.concatenate([v[:, :, :2], wrapped[:, :, :2]], axis=2)
    x_low = shifted_in(upward, "gx", 1)
    x_high = shifted_in(downward, "gx", -1)
    z_pad = ((0, 0), (2, 2), (0, 0), (0, 0))
    xe = jnp.pad(jnp.concatenate([x_low[:, :, :2], v, x_high[:, :, :2]], axis=2), z_pad)
    fe = jnp.pad(jnp.concatenate([x_low[:, :, 2:], wrapped, x_high[:, :, 2:]], axis=2), z_pad)
    return xe, fe


def full_pad(xe, fe):
    wide_y = xe.shape[-1]
    return jnp.concatenate([fe[..., wide_y - 2 :], xe, fe[..., :2]], axis=-1)


def window(array_in, move_z, move_x, move_y):
    size_z = array_in.shape[-3] - 4
    size_x = array_in.shape[-2] - 4
    size_y = array_in.shape[-1] - 4
    return array_in[
        ...,
        2 + move_z : 2 + move_z + size_z,
        2 + move_x : 2 + move_x + size_x,
        2 + move_y : 2 + move_y + size_y,
    ]


def placement(starts, slots, wide):
    source = lax.broadcasted_iota(jnp.int32, (slots, wide, 2 * wide), 1)
    target = lax.broadcasted_iota(jnp.int32, (slots, wide, 2 * wide), 2)
    return (target == source + starts.astype(jnp.int32)[:, None, None]).astype(jnp.float32)


def blend_home(patches, patch_wx, patch_wy, offset_x, offset_y, live_count):
    slots, depth_z, wide_x, wide_y = patches.shape
    slot_ids = lax.broadcasted_iota(jnp.int32, (slots,), 0)
    live = (slot_ids < live_count[0, 0]).astype(jnp.float32)
    place_x = placement(offset_x[:, 0, 0], slots, wide_x)
    place_y = placement(offset_y[:, 0, 0], slots, wide_y)
    along_x = patch_wx[:, 0, :].astype(jnp.float32) * live[:, None]
    along_y = patch_wy[:, 0, :].astype(jnp.float32)
    scaled = patches.astype(jnp.float32) * along_x[:, None, :, None] * along_y[:, None, None, :]
    wide_rows = jnp.einsum("szxy,syY->szxY", scaled, place_y, precision=EXACT)
    weighted = jnp.einsum("szxY,sxX->zXY", wide_rows, place_x, precision=EXACT)
    row_weight = jnp.einsum("sx,sxX->sX", along_x, place_x, precision=EXACT)
    col_weight = jnp.einsum("sy,syY->sY", along_y, place_y, precision=EXACT)
    weight_sum = jnp.einsum("sX,sY->XY", row_weight, col_weight, precision=EXACT)
    return (weighted, weight_sum)


def relax_kernel(xe_ref, fe_ref, mc_ref, bc_ref, rate_ref, force_ref, out_ref):
    chunk = out_ref.shape[1]
    wide_x = out_ref.shape[2]
    wide_y = out_ref.shape[3]
    first = pl.program_id(0) * chunk
    lane = lax.broadcasted_iota(jnp.int32, (HALF, wide_y), 1)
    inside = {dy: (lane + dy >= 0) & (lane + dy < wide_y) for dy in (-2, -1, 1, 2)}

    def body(z, carry):
        plane = first + z + 2
        for half in range(wide_x // HALF):
            rows = pl.ds(half * HALF, HALF)
            rate = rate_ref[z, rows, :]
            for comp in range(3):
                cache = {}

                def val(c, dz, dx, dy):
                    key = (c, dz, dx, dy)
                    if key not in cache:
                        span = pl.ds(2 + dx + half * HALF, HALF)
                        got = xe_ref[c, plane + dz, span, :]
                        if dy != 0:
                            ring = fe_ref[c, plane + dz, span, :]
                            turn = (-dy) % wide_y
                            got = jnp.where(
                                inside[dy], pltpu.roll(got, turn, 1), pltpu.roll(ring, turn, 1)
                            )
                        cache[key] = got
                    return cache[key]

                centre = val(comp, 0, 0, 0)
                laplace = 0.0
                for dim in range(3):
                    ahead = STEPS_UNIT[dim]
                    behind = tuple(-t for t in ahead)
                    laplace = laplace + mc_ref[2 * dim, z, rows, :] * (val(comp, *ahead) - centre)
                    laplace = laplace - mc_ref[2 * dim + 1, z, rows, :] * (
                        centre - val(comp, *behind)
                    )
                step = STEPS_UNIT[comp]

                def divergence(sign):
                    result = 0.0
                    for dim in range(3):
                        unit = STEPS_UNIT[dim]
                        fwd = tuple(sign * step[k] + unit[k] for k in range(3))
                        bwd = tuple(sign * step[k] - unit[k] for k in range(3))
                        result = result + 0.5 * (val(dim, *fwd) - val(dim, *bwd))
                    return result

                grad_div = 0.5 * (
                    bc_ref[2 * comp, z, rows, :] * divergence(1)
                    - bc_ref[2 * comp + 1, z, rows, :] * divergence(-1)
                )
                out_ref[comp, z, rows, :] = centre + rate * (
                    laplace + grad_div + force_ref[comp, z, rows, :]
                )
        return carry

    lax.fori_loop(0, chunk, body, 0)


def relax_call(xe, fe, mc, bc, rate, forcing, chunk=16):
    chans, depth, wide_x, wide_y = forcing.shape
    out_shape = jax.ShapeDtypeStruct(forcing.shape, jnp.float32)
    moved = sum(a.size * a.dtype.itemsize for a in (xe, fe, mc, bc, rate, forcing)) + forcing.size * 4
    whole = pl.BlockSpec(xe.shape, lambda g: (0, 0, 0, 0))
    six = pl.BlockSpec((mc.shape[0], chunk, wide_x, wide_y), lambda g: (0, g, 0, 0))
    three = pl.BlockSpec((chans, chunk, wide_x, wide_y), lambda g: (0, g, 0, 0))
    one = pl.BlockSpec((chunk, wide_x, wide_y), lambda g: (g, 0, 0))
    return pl.pallas_call(
        relax_kernel,
        out_shape=out_shape,
        grid=(depth // chunk,),
        in_specs=[whole, whole, six, six, one, three],
        out_specs=three,
        compiler_params=pltpu.CompilerParams(vmem_limit_bytes=48 * 1024 * 1024),
        cost_estimate=pl.CostEstimate(
            flops=forcing.size * 70, transcendentals=0, bytes_accessed=moved
        ),
    )(xe, fe, mc, bc, rate, forcing)


def per_device(
    patches,
    patch_wx,
    patch_wy,
    offset_x,
    offset_y,
    block_counts,
    template,
    stiff_mu,
    stiff_lam,
    start_field,
):
    wide_x = patches.shape[2]
    wide_y = patches.shape[3]
    canvas, canvas_weight = blend_home(patches, patch_wx, patch_wy, offset_x, offset_y, block_counts)

    def quarter(upper_x, upper_y):
        cut_x = slice(upper_x * wide_x, (upper_x + 1) * wide_x)
        cut_y = slice(upper_y * wide_y, (upper_y + 1) * wide_y)
        return jnp.concatenate([canvas[:, cut_x, cut_y], canvas_weight[None, cut_x, cut_y]], axis=0)

    from_y = shifted_in(quarter(0, 1), "gy", 1)
    from_x = shifted_in(quarter(1, 0), "gx", 1)
    from_xy = diagonal_in(quarter(1, 1))
    total = quarter(0, 0) + from_y + from_x + from_xy
    weighted = total[:-1]
    weight_sum = total[-1]
    joined = (weighted / jnp.maximum(weight_sum, 1.0)[None]).astype(jnp.bfloat16)

    bulk = stiff_lam + stiff_mu
    rate = RELAX_FACTOR / (6.0 * stiff_mu + 3.0 * bulk)
    moduli = full_pad(*halo(jnp.stack([stiff_mu, bulk])))
    shear = moduli[0]
    bulk_pad = moduli[1]
    shear_here = window(shear, 0, 0, 0)
    mean_shear = []
    bulk_beside = []
    for dim in range(3):
        ahead = STEPS_UNIT[dim]
        behind = tuple(-t for t in ahead)
        mean_shear.append(0.5 * (shear_here + window(shear, *ahead)))
        mean_shear.append(0.5 * (shear_here + window(shear, *behind)))
        bulk_beside.append(window(bulk_pad, *ahead))
        bulk_beside.append(window(bulk_pad, *behind))
    mean_shear = jnp.stack(mean_shear)
    bulk_beside = jnp.stack(bulk_beside)

    image = full_pad(*halo(joined[None].astype(jnp.float32)))[0]
    centre = window(image, 0, 0, 0)
    mismatch = template.astype(jnp.float32) - centre
    slopes = []
    for dim in range(3):
        ahead = STEPS_UNIT[dim]
        behind = tuple(-t for t in ahead)
        slopes.append(0.5 * (window(image, *ahead) - window(image, *behind)) * mismatch)
    forcing = jnp.stack(slopes)

    def one_pass(pass_idx, field):
        xe, fe = halo(field)
        return relax_call(xe, fe, mean_shear, bulk_beside, rate, forcing)

    field = lax.fori_loop(0, PASSES, one_pass, start_field)
    return (joined, field)


def solution(mesh):
    placed = (
        P(None, None, "gx", "gy"),
        P(None, "gy", "gx"),
        P(None, "gx", "gy"),
        P(None, "gx", "gy"),
        P(None, "gx", "gy"),
        P("gx", "gy"),
        P(None, "gx", "gy"),
        P(None, "gx", "gy"),
        P(None, "gx", "gy"),
        P(None, None, "gx", "gy"),
    )
    return jax.shard_map(
        per_device,
        mesh=mesh,
        in_specs=placed,
        out_specs=(P(None, "gx", "gy"), P(None, None, "gx", "gy")),
        check_vma=False,
    )
```
